512 devices in a mesh: ep: 128 (over z, x, core), rep: 4 (over y).
Axes of the slice: x: 4, y: 4, z: 16, core: 2. Of those that a mesh axis runs over, the one named last changes fastest.
Arguments:
- tokens: bfloat16 [65536, 2048], P(('ep', 'rep')), may hold values from -6 to 6
- cotangent: bfloat16 [65536, 2048], P(('ep', 'rep')), may hold values from -6 to 6
- expert_ids: int32 [65536, 2], P(('ep', 'rep')), may hold values from 0 to 63, all different within a row; in each aligned block of 128 rows (0 to 127, 128 to 255, ...) at most 5 rows name the same one
- gate_values: float32 [65536, 2], P(('ep', 'rep')), may hold values from 0.1 to 1
- up_weight: bfloat16 [2048, 81920], P('rep', 'ep'), may hold values from -0.125 to 0.125
- down_weight: bfloat16 [81920, 2048], P('ep', 'rep'), may hold values from -0.15625 to 0.15625
Outputs:
- token_grad: bfloat16 [65536, 2048], P(('ep', 'rep'))
- gate_grad: float32 [65536, 2], P(('ep', 'rep'))
- down_grad: bfloat16 [81920, 2048], P('ep', 'rep')
The draws below stay inside these ranges and needn't reach their ends.
Inputs may be any that keep to these rules, and one draw needn't show every extreme that they name: `expert_ids`: each token names two different experts; among the 256 assignments of one device's tokens at most 5 name the same expert, a bound that is reached in some blocks.
All inputs are finite; a program needn't handle non-finite values.
Results may differ from the reference program's by a relative error of at most 0.02.
Values may be sent and summed in bfloat16 or wider, within the bound.
No kernel may reach another device: no remote copies, remote signals or barrier semaphores. Data moves between devices by JAX's collectives and lax.ppermute only.
A program may use at most 128 MiB of HBM per device.

```python
import math
import jax
import jax.numpy as jnp
import numpy as np
from jax import lax

D = 2048
HIDDEN_SIZE = 1280
TOK_DEV = 128
EXPERTS = 64
CAP = 5
TOKENS = 65536
N_EP = 128
N_REP = 4


def block_levels(key, shape, split, low, top_value):
    def one(dim, blocks):
        steps = jax.random.uniform(jax.random.fold_in(jax.random.fold_in(key, 6), dim), (blocks,), jnp.float32, low / len(split), top_value / len(split))
        return jnp.repeat(jnp.exp(steps), shape[dim] // blocks).reshape((-1,) + (1,) * (len(shape) - dim - 1))

    factor_of = one(*split[0])
    for cut in split[1:]:
        factor_of = factor_of * one(*cut)
    return factor_of


def routed_block(key, own, number, rows, number_of, top, limit, lean):
    sequence = jax.random.permutation(key, number_of)
    heavy_load, common = load_shares(number_of, rows * top, limit, lean, True), load_shares(number_of, rows * top, limit, lean, False)
    places = jnp.arange(number_of)

    def named(tallies, rotation):
        used = int((tallies > 0).sum())
        fixed = max(1, used // 4)
        moved = fixed + (places - fixed + rotation * (used - fixed)) % max(1, number_of - fixed)
        return jnp.zeros((number_of,), jnp.int32).at[sequence[jnp.where(places < fixed, places, moved)]].set(jnp.asarray(tallies, jnp.int32))

    tallies = jnp.where(number % 4 == 0, named(heavy_load, number // 4), named(common, number - number // 4 - 1))
    mixed = jax.random.permutation(jax.random.fold_in(own, 3), number_of)
    source_of, sink = mixed[0:number_of // 2 * 2:2], mixed[1:number_of // 2 * 2:2]
    slack = jnp.minimum(tallies[source_of] - 1, limit - tallies[sink]) // 2
    slack = jnp.where((source_of == sequence[0]) | (sink == sequence[0]) | (tallies[sink] == 0), 0, jnp.maximum(slack, 0))
    moved = jax.random.randint(jax.random.fold_in(own, 4), (number_of // 2,), 0, 1 << 20) % (slack + 1)
    tallies = tallies.at[source_of].add(-moved).at[sink].add(moved)
    items = jnp.searchsorted(jnp.cumsum(tallies), jnp.arange(rows * top), side="right").astype(jnp.int32)
    grid = items.reshape(top, rows).T
    grid = grid[jax.random.permutation(jax.random.fold_in(own, 1), rows)]
    rotation = jax.random.randint(jax.random.fold_in(own, 2), (rows, 1), 0, top)
    return jnp.take_along_axis(grid, (jnp.arange(top)[None, :] + rotation) % top, axis=1)


def load_shares(count, total, limit, skew, full):
    weights = [(1 << 20) // math.isqrt(rank ** skew) + 1 for rank in range(1, count + 1)]
    largest = limit if full else min(limit, max(-(-total // count), total * weights[0] // sum(weights)))
    least = 1 if total - largest >= count - 1 else 0
    holding, surplus = [largest] + [least] * (count - 1), total - largest - least * (count - 1)
    while surplus > 0:
        free = [i for i in range(1, count) if holding[i] < largest] or [i for i in range(1, count) if holding[i] < limit]
        whole, remaining = sum([weights[i] for i in free]), surplus
        for i in free:
            addition = min(limit - holding[i], max(1, remaining * weights[i] // whole), surplus)
            holding[i] = holding[i] + addition
            surplus = surplus - addition
    return np.array(holding)


def scatter_about(stream_key, dims, scale, limit, pieces=(), kind=jnp.bfloat16):
    array = jax.random.normal(stream_key, dims, jnp.float32) * scale
    if len(pieces) > 0:
        array = block_levels(stream_key, dims, pieces, -0.22, 0.18) * array
    return jnp.clip(array, min=-limit, max=limit).astype(kind)


def setup_inputs(seed: int = 0) -> dict:
    keys = jax.random.split(jax.random.key(seed), 7)
    tokens = scatter_about(keys[0], (TOKENS, D), 1.0, 6.0, ((0, 512),))
    cotangent = scatter_about(keys[1], (TOKENS, D), 1.0, 6.0, ((0, 512),))
    expert_ids_keys = jax.random.split(jax.random.fold_in(keys[2], 1), TOKENS // TOK_DEV)
    expert_ids_turns = jax.random.permutation(jax.random.fold_in(keys[2], 3), TOKENS // TOK_DEV)
    expert_ids = jax.vmap(lambda own, number: routed_block(jax.random.fold_in(keys[2], 2), own, number, TOK_DEV, EXPERTS, 2, CAP, 1))(expert_ids_keys, expert_ids_turns).reshape((TOKENS, 2))
    gate_values = jnp.clip(0.1 + 0.9 * jax.random.uniform(keys[3], (TOKENS, 2), jnp.float32) ** block_levels(keys[3], (TOKENS, 2), ((0, 512),), -0.2, 0.2), 0.1, 1.0)
    up_weight = scatter_about(keys[4], (D, EXPERTS * HIDDEN_SIZE), D ** -0.5, 0.125, ((0, 4), (1, 128)))
    down_weight = scatter_about(keys[5], (EXPERTS * HIDDEN_SIZE, D), HIDDEN_SIZE ** -0.5, 0.15625, ((0, 128), (1, 4)))
    return {"tokens": tokens, "cotangent": cotangent, "expert_ids": expert_ids, "gate_values": gate_values, "up_weight": up_weight, "down_weight": down_weight}


tanh_scale = math.sqrt(2.0 / math.pi)
cubic_coef = 0.044715

def gelu_tanh(argument):
    inner_arg = tanh_scale * (argument + cubic_coef * argument * argument * argument)
    return 0.5 * argument * (1.0 + jnp.tanh(inner_arg))

def gelu_slope(argument):
    tanh_value = jnp.tanh(tanh_scale * (argument + cubic_coef * argument * argument * argument))
    return 0.5 * (1.0 + tanh_value) + 0.5 * argument * (1.0 - tanh_value * tanh_value) * tanh_scale * (1.0 + 3.0 * cubic_coef * argument * argument)

def reference(tokens, cotangent, expert_ids, gate_values, up_weight, down_weight):
    blocks = N_EP * N_REP
    per_block = 2 * TOK_DEV
    flat_ids = expert_ids.reshape(blocks, per_block)
    onehot = (flat_ids[:, :, None] == jnp.arange(EXPERTS, dtype=jnp.int32)[None, None, :]).astype(jnp.int32)
    running_rank = jnp.cumsum(onehot, axis=1)
    slot_index = lax.optimization_barrier(jnp.sum(onehot * running_rank, axis=2)) - 1
    block_ids = jnp.arange(blocks, dtype=jnp.int32)[:, None]
    position = flat_ids * (blocks * CAP) + block_ids * CAP + slot_index
    slot_table = jnp.full((EXPERTS * blocks * CAP,), -1, jnp.int32)
    slot_table = slot_table.at[position.reshape(-1)].set(jnp.arange(blocks * per_block, dtype=jnp.int32))
    slot_table = slot_table.reshape(EXPERTS, blocks * CAP)
    gate_flat = gate_values.reshape(-1)
    half_units = HIDDEN_SIZE // 2
    contract_last = (((1,), (1,)), ((), ()))

    def per_expert(running, inputs):
        token_acc, gate_acc = running
        expert, where_from = inputs
        is_valid = where_from >= 0
        assign = jnp.where(is_valid, where_from, 0).astype(jnp.int32)
        token_index = (assign // 2).astype(jnp.int32)
        rows_x = jnp.where(is_valid[:, None], tokens[token_index], jnp.zeros((), tokens.dtype))
        rows_dy = jnp.where(is_valid[:, None], cotangent[token_index], jnp.zeros((), cotangent.dtype))
        rows_gate = jnp.where(is_valid, gate_flat[assign], jnp.zeros((), gate_flat.dtype))
        up_block = lax.dynamic_slice_in_dim(up_weight, (expert * HIDDEN_SIZE).astype(jnp.int32), HIDDEN_SIZE, 1)
        down_block = lax.dynamic_slice_in_dim(down_weight, (expert * HIDDEN_SIZE).astype(jnp.int32), HIDDEN_SIZE, 0)
        pre_act = jnp.dot(rows_x, up_block, preferred_element_type=jnp.float32)
        hidden = gelu_tanh(pre_act)
        hidden_bf = hidden.astype(jnp.bfloat16)
        grad_hidden = lax.dot_general(rows_dy, down_block, contract_last, preferred_element_type=jnp.float32)
        products = hidden * grad_hidden
        gate_part = lax.optimization_barrier(jnp.sum(products[:, :half_units], axis=1)) + lax.optimization_barrier(jnp.sum(products[:, half_units:], axis=1))
        scaled_dy = (rows_gate[:, None] * rows_dy.astype(jnp.float32)).astype(jnp.bfloat16)
        grad_pre = (rows_gate[:, None] * grad_hidden * gelu_slope(pre_act)).astype(jnp.bfloat16)
        first_half = lax.dot_general(grad_pre[:, :half_units], up_block[:, :half_units], contract_last, preferred_element_type=jnp.float32).astype(jnp.bfloat16)
        second_half = lax.dot_general(grad_pre[:, half_units:], up_block[:, half_units:], contract_last, preferred_element_type=jnp.float32).astype(jnp.bfloat16)
        token_part = first_half.astype(jnp.float32) + second_half.astype(jnp.float32)
        token_acc = token_acc.at[token_index].add(jnp.where(is_valid[:, None], token_part, jnp.zeros((), token_part.dtype)))
        gate_acc = gate_acc.at[assign].add(jnp.where(is_valid, gate_part, jnp.zeros((), gate_part.dtype)))
        hidden_rep = hidden_bf.reshape(N_EP, N_REP, CAP, HIDDEN_SIZE).transpose(1, 0, 2, 3).reshape(N_REP, N_EP * CAP, HIDDEN_SIZE).astype(jnp.float32)
        scaled_rep = scaled_dy.reshape(N_EP, N_REP, CAP, D).transpose(1, 0, 2, 3).reshape(N_REP, N_EP * CAP, D).astype(jnp.float32)
        partial_value = jnp.einsum('rnh,rnd->rhd', hidden_rep, scaled_rep)
        rounded = lax.optimization_barrier(partial_value.astype(jnp.bfloat16))
        down_part = lax.optimization_barrier(jnp.sum(rounded.astype(jnp.float32), axis=0)).astype(jnp.bfloat16)
        return ((token_acc, gate_acc), down_part)
    start_state = (jnp.zeros((TOKENS, D), jnp.float32), jnp.zeros((TOKENS * 2,), jnp.float32))
    final_state, down_parts = lax.scan(per_expert, start_state, (jnp.arange(EXPERTS, dtype=jnp.int32), slot_table))
    token_grad = final_state[0].astype(jnp.bfloat16)
    gate_grad = final_state[1].reshape(TOKENS, 2)
    down_grad = down_parts.reshape(EXPERTS * HIDDEN_SIZE, D)
    return (token_grad, gate_grad, down_grad)
```

```python
import math

import jax
import jax.numpy as jnp
from jax import lax
from jax.sharding import Mesh
from jax.sharding import PartitionSpec as P

tanh_scale = math.sqrt(2.0 / math.pi)
cubic_coef = 0.044715
EXTRA = 128


def gelu_tanh(argument):
    inner_arg = tanh_scale * (argument + cubic_coef * argument * argument * argument)
    return 0.5 * argument * (1.0 + jnp.tanh(inner_arg))


def gelu_slope(argument):
    tanh_value = jnp.tanh(tanh_scale * (argument + cubic_coef * argument * argument * argument))
    return 0.5 * (1.0 + tanh_value) + 0.5 * argument * (
        1.0 - tanh_value * tanh_value
    ) * tanh_scale * (1.0 + 3.0 * cubic_coef * argument * argument)


def split_bf16(value):
    high = value.astype(jnp.bfloat16)
    low = (value - high.astype(jnp.float32)).astype(jnp.bfloat16)
    return high, low


def expert_terms(rows_x, rows_dy, rows_gate, up_weight, down_weight):
    contract_last = (((1,), (1,)), ((), ()))
    up_full = lax.all_gather(up_weight, "rep", axis=0, tiled=True)
    down_full = lax.all_gather(down_weight, "rep", axis=1, tiled=True)
    pre_act = jnp.dot(rows_x, up_full, preferred_element_type=jnp.float32)
    grad_hidden = lax.dot_general(
        rows_dy, down_full, contract_last, preferred_element_type=jnp.float32
    )
    hidden = gelu_tanh(pre_act)
    hidden_bf = hidden.astype(jnp.bfloat16)
    gate_part = jnp.sum(hidden * grad_hidden, axis=1)
    scaled_dy = (rows_gate[:, None] * rows_dy.astype(jnp.float32)).astype(jnp.bfloat16)
    down_term = lax.dot_general(
        hidden_bf, scaled_dy, (((0,), (0,)), ((), ())), preferred_element_type=jnp.float32
    ).astype(jnp.bfloat16)
    down_sum = (
        lax.psum_scatter(down_term, "rep", scatter_dimension=1, tiled=True)
        .astype(jnp.float32)
        .astype(jnp.bfloat16)
    )
    grad_pre = (rows_gate[:, None] * grad_hidden * gelu_slope(pre_act)).astype(jnp.bfloat16)
    token_part = lax.dot_general(
        grad_pre, up_full, contract_last, preferred_element_type=jnp.float32
    ).astype(jnp.bfloat16)
    return (token_part, gate_part, down_sum)


def local(tokens, cotangent, expert_ids, gate_values, up_weight, down_weight):
    experts = lax.axis_size("epc")
    cores = lax.axis_size("core")
    core = lax.axis_index("core")
    tok_rows, width = tokens.shape
    capacity = 5 * tok_rows // (2 * experts)
    assignments = 2 * tok_rows
    flat_ids = expert_ids.reshape(-1)
    onehot = (flat_ids[:, None] == jnp.arange(experts, dtype=jnp.int32)[None, :]).astype(jnp.int32)
    running_rank = jnp.cumsum(onehot, axis=0)
    slot_index = jnp.sum(onehot * running_rank, axis=1) - 1
    position = flat_ids * capacity + slot_index
    where_from = (
        jnp.full((experts * capacity,), -1, jnp.int32)
        .at[position]
        .set(jnp.arange(assignments, dtype=jnp.int32))
    )
    is_valid = where_from >= 0
    assign = jnp.where(is_valid, where_from, 0)
    token_index = assign // 2
    send_x = jnp.where(is_valid[:, None], tokens[token_index], jnp.zeros((), tokens.dtype))
    send_dy = jnp.where(is_valid[:, None], cotangent[token_index], jnp.zeros((), cotangent.dtype))
    send_gate = jnp.where(is_valid, gate_values.reshape(-1)[assign], 0.0)
    gate_high, gate_low = split_bf16(send_gate)
    lane = jnp.arange(EXTRA, dtype=jnp.int32)[None, :]
    extra = jnp.where(
        lane == 0, gate_high[:, None], jnp.where(lane == 1, gate_low[:, None], jnp.zeros((), jnp.bfloat16))
    )
    send = jnp.concatenate([send_x, send_dy, extra], axis=1).reshape(experts, capacity, -1)
    arrived = lax.all_to_all(send, "epc", split_axis=0, concat_axis=0, tiled=True)
    both = lax.all_gather(arrived, "core", axis=0, tiled=False)
    rows = both.reshape(cores * experts * capacity, -1)
    rows_gate = rows[:, 2 * width].astype(jnp.float32) + rows[:, 2 * width + 1].astype(jnp.float32)
    token_part, gate_part, down_sum = expert_terms(
        rows[:, :width], rows[:, width : 2 * width], rows_gate, up_weight, down_weight
    )
    part_high, part_low = split_bf16(gate_part)
    back_lane = jnp.arange(EXTRA, dtype=jnp.int32)[None, :]
    back_extra = jnp.where(
        back_lane == 2 * core,
        part_high[:, None],
        jnp.where(back_lane == 2 * core + 1, part_low[:, None], jnp.zeros((), jnp.bfloat16)),
    )
    back = jnp.concatenate([token_part, back_extra], axis=1).reshape(cores, experts * capacity, -1)
    summed = lax.psum_scatter(back, "core", scatter_dimension=0, tiled=False)
    returned = lax.all_to_all(
        summed.reshape(experts, capacity, -1), "epc", split_axis=0, concat_axis=0, tiled=True
    ).reshape(experts * capacity, -1)
    picked = returned[position].astype(jnp.float32)
    token_grad = jnp.sum(picked[:, :width].reshape(tok_rows, 2, width), axis=1).astype(jnp.bfloat16)
    gate_grad = (
        (picked[:, width] + picked[:, width + 1]) + (picked[:, width + 2] + picked[:, width + 3])
    ).reshape(tok_rows, 2)
    return (token_grad, gate_grad, down_sum)


def solution(mesh):
    ep_size = mesh.shape["ep"]
    split_mesh = Mesh(
        mesh.devices.reshape(ep_size // 2, 2, mesh.shape["rep"]), ("epc", "core", "rep")
    )
    ep = ("epc", "core")
    return jax.shard_map(
        local,
        mesh=split_mesh,
        in_specs=(
            P(ep + ("rep",), None),
            P(ep + ("rep",), None),
            P(ep + ("rep",), None),
            P(ep + ("rep",), None),
            P("rep", ep),
            P(ep, "rep"),
        ),
        out_specs=(P(ep + ("rep",), None), P(ep + ("rep",), None), P(ep, "rep")),
        check_vma=False,
    )
```

```python
import math

import jax
import jax.numpy as jnp
from jax import lax
from jax.sharding import Mesh
from jax.sharding import PartitionSpec as P

tanh_scale = math.sqrt(2.0 / math.pi)
cubic_coef = 0.044715
EXTRA = 128
LANES = 128


def gelu_tanh(argument):
    inner_arg = tanh_scale * (argument + cubic_coef * argument * argument * argument)
    return 0.5 * argument * (1.0 + jnp.tanh(inner_arg))


def gelu_slope(argument):
    tanh_value = jnp.tanh(tanh_scale * (argument + cubic_coef * argument * argument * argument))
    return 0.5 * (1.0 + tanh_value) + 0.5 * argument * (
        1.0 - tanh_value * tanh_value
    ) * tanh_scale * (1.0 + 3.0 * cubic_coef * argument * argument)


def split_bf16(value):
    high = value.astype(jnp.bfloat16)
    low = (value - high.astype(jnp.float32)).astype(jnp.bfloat16)
    return high, low


def expert_terms(rows_x, rows_dy, rows_gate, up_weight, down_weight):
    contract_last = (((1,), (1,)), ((), ()))
    up_full = lax.all_gather(up_weight, "rep", axis=0, tiled=True)
    down_full = lax.all_gather(down_weight, "rep", axis=1, tiled=True)
    pre_act = jnp.dot(rows_x, up_full, preferred_element_type=jnp.float32)
    grad_hidden = lax.dot_general(
        rows_dy, down_full, contract_last, preferred_element_type=jnp.float32
    )
    hidden = gelu_tanh(pre_act)
    hidden_bf = hidden.astype(jnp.bfloat16)
    gate_part = jnp.sum(hidden * grad_hidden, axis=1)
    scaled_dy = (rows_gate[:, None] * rows_dy.astype(jnp.float32)).astype(jnp.bfloat16)
    down_term = lax.dot_general(
        hidden_bf, scaled_dy, (((0,), (0,)), ((), ())), preferred_element_type=jnp.float32
    ).astype(jnp.bfloat16)
    down_sum = (
        lax.psum_scatter(down_term, "rep", scatter_dimension=1, tiled=True)
        .astype(jnp.float32)
        .astype(jnp.bfloat16)
    )
    grad_pre = (rows_gate[:, None] * grad_hidden * gelu_slope(pre_act)).astype(jnp.bfloat16)
    token_part = lax.dot_general(
        grad_pre, up_full, contract_last, preferred_element_type=jnp.float32
    ).astype(jnp.bfloat16)
    return (token_part, gate_part, down_sum)


def local(tokens, cotangent, expert_ids, gate_values, up_weight, down_weight):
    experts = lax.axis_size("epc")
    tok_rows, width = tokens.shape
    capacity = 5 * tok_rows // (2 * experts)
    assignments = 2 * tok_rows
    flat_ids = expert_ids.reshape(-1)
    onehot = (flat_ids[:, None] == jnp.arange(experts, dtype=jnp.int32)[None, :]).astype(jnp.int32)
    running_rank = jnp.cumsum(onehot, axis=0)
    slot_index = jnp.sum(onehot * running_rank, axis=1) - 1
    position = flat_ids * capacity + slot_index
    where_from = (
        jnp.full((experts * capacity,), -1, jnp.int32)
        .at[position]
        .set(jnp.arange(assignments, dtype=jnp.int32))
    )
    is_valid = where_from >= 0
    assign = jnp.where(is_valid, where_from, 0)
    token_index = assign // 2
    send_x = jnp.where(is_valid[:, None], tokens[token_index], jnp.zeros((), tokens.dtype))
    send_dy = jnp.where(is_valid[:, None], cotangent[token_index], jnp.zeros((), cotangent.dtype))
    send_gate = jnp.where(is_valid, gate_values.reshape(-1)[assign], 0.0)
    gate_high, gate_low = split_bf16(send_gate)
    lane = jnp.arange(EXTRA, dtype=jnp.int32)[None, :]
    extra = jnp.where(
        lane == 0, gate_high[:, None], jnp.where(lane == 1, gate_low[:, None], jnp.zeros((), jnp.bfloat16))
    )
    send = jnp.concatenate([send_x, send_dy, extra], axis=1)
    row_width = send.shape[1]
    arrived = lax.all_to_all(
        send.reshape(experts, capacity * row_width // LANES, LANES),
        "epc",
        split_axis=0,
        concat_axis=0,
        tiled=True,
    ).reshape(experts * capacity, row_width)
    swap = [(0, 1), (1, 0)]
    partner_rows = lax.ppermute(arrived, "core", swap)
    rows = jnp.concatenate([arrived, partner_rows], axis=0)
    rows_gate = rows[:, 2 * width].astype(jnp.float32) + rows[:, 2 * width + 1].astype(jnp.float32)
    token_part, gate_part, down_sum = expert_terms(
        rows[:, :width], rows[:, width : 2 * width], rows_gate, up_weight, down_weight
    )
    own = experts * capacity
    part_high, part_low = split_bf16(gate_part[own:])
    back_lane = jnp.arange(EXTRA, dtype=jnp.int32)[None, :]
    back_extra = jnp.where(
        back_lane == 0,
        part_high[:, None],
        jnp.where(back_lane == 1, part_low[:, None], jnp.zeros((), jnp.bfloat16)),
    )
    partner_back = lax.ppermute(
        jnp.concatenate([token_part[own:], back_extra], axis=1), "core", swap
    )
    token_sum = (
        token_part[:own].astype(jnp.float32) + partner_back[:, :width].astype(jnp.float32)
    ).astype(jnp.bfloat16)
    gate_sum = gate_part[:own] + (
        partner_back[:, width].astype(jnp.float32) + partner_back[:, width + 1].astype(jnp.float32)
    )
    sum_high, sum_low = split_bf16(gate_sum)
    ret_extra = jnp.where(
        back_lane == 0,
        sum_high[:, None],
        jnp.where(back_lane == 1, sum_low[:, None], jnp.zeros((), jnp.bfloat16)),
    )
    back = jnp.concatenate([token_sum, ret_extra], axis=1)
    back_width = back.shape[1]
    returned = lax.all_to_all(
        back.reshape(experts, capacity * back_width // LANES, LANES),
        "epc",
        split_axis=0,
        concat_axis=0,
        tiled=True,
    ).reshape(experts * capacity, back_width)
    picked = returned[position].astype(jnp.float32)
    token_grad = jnp.sum(picked[:, :width].reshape(tok_rows, 2, width), axis=1).astype(jnp.bfloat16)
    gate_grad = (picked[:, width] + picked[:, width + 1]).reshape(tok_rows, 2)
    return (token_grad, gate_grad, down_sum)


def solution(mesh):
    ep_size = mesh.shape["ep"]
    split_mesh = Mesh(
        mesh.devices.reshape(ep_size // 2, 2, mesh.shape["rep"]), ("epc", "core", "rep")
    )
    ep = ("epc", "core")
    return jax.shard_map(
        local,
        mesh=split_mesh,
        in_specs=(
            P(ep + ("rep",), None),
            P(ep + ("rep",), None),
            P(ep + ("rep",), None),
            P(ep + ("rep",), None),
            P("rep", ep),
            P(ep, "rep"),
        ),
        out_specs=(P(ep + ("rep",), None), P(ep + ("rep",), None), P(ep, "rep")),
        check_vma=False,
    )
```

```python
import math

import jax
import jax.numpy as jnp
from jax import lax
from jax.sharding import Mesh
from jax.sharding import PartitionSpec as P

tanh_scale = math.sqrt(2.0 / math.pi)
cubic_coef = 0.044715
EXTRA = 128
LANES = 128


def gelu_tanh(argument):
    inner_arg = tanh_scale * (argument + cubic_coef * argument * argument * argument)
    return 0.5 * argument * (1.0 + jnp.tanh(inner_arg))


def gelu_slope(argument):
    tanh_value = jnp.tanh(tanh_scale * (argument + cubic_coef * argument * argument * argument))
    return 0.5 * (1.0 + tanh_value) + 0.5 * argument * (
        1.0 - tanh_value * tanh_value
    ) * tanh_scale * (1.0 + 3.0 * cubic_coef * argument * argument)


def split_bf16(value):
    high = value.astype(jnp.bfloat16)
    low = (value - high.astype(jnp.float32)).astype(jnp.bfloat16)
    return high, low


def expert_terms(rows_x, rows_dy, rows_gate, up_weight, down_weight):
    contract_last = (((1,), (1,)), ((), ()))
    both_full = lax.all_gather(
        jnp.stack([up_weight, down_weight.T]), "rep", axis=1, tiled=True
    )
    up_full = both_full[0]
    pre_act = jnp.dot(rows_x, up_full, preferred_element_type=jnp.float32)
    grad_hidden = jnp.dot(rows_dy, both_full[1], preferred_element_type=jnp.float32)
    hidden = gelu_tanh(pre_act)
    hidden_bf = hidden.astype(jnp.bfloat16)
    gate_part = jnp.sum(hidden * grad_hidden, axis=1)
    scaled_dy = (rows_gate[:, None] * rows_dy.astype(jnp.float32)).astype(jnp.bfloat16)
    down_term = lax.dot_general(
        hidden_bf, scaled_dy, (((0,), (0,)), ((), ())), preferred_element_type=jnp.float32
    ).astype(jnp.bfloat16)
    down_sum = (
        lax.psum_scatter(down_term, "rep", scatter_dimension=1, tiled=True)
        .astype(jnp.float32)
        .astype(jnp.bfloat16)
    )
    grad_pre = (rows_gate[:, None] * grad_hidden * gelu_slope(pre_act)).astype(jnp.bfloat16)
    token_part = lax.dot_general(
        grad_pre, up_full, contract_last, preferred_element_type=jnp.float32
    ).astype(jnp.bfloat16)
    return (token_part, gate_part, down_sum)


def local(tokens, cotangent, expert_ids, gate_values, up_weight, down_weight):
    experts = lax.axis_size("epc")
    tok_rows, width = tokens.shape
    capacity = 5 * tok_rows // (2 * experts)
    assignments = 2 * tok_rows
    flat_ids = expert_ids.reshape(-1)
    onehot = (flat_ids[:, None] == jnp.arange(experts, dtype=jnp.int32)[None, :]).astype(jnp.int32)
    running_rank = jnp.cumsum(onehot, axis=0)
    slot_index = jnp.sum(onehot * running_rank, axis=1) - 1
    position = flat_ids * capacity + slot_index
    where_from = (
        jnp.full((experts * capacity,), -1, jnp.int32)
        .at[position]
        .set(jnp.arange(assignments, dtype=jnp.int32))
    )
    is_valid = where_from >= 0
    assign = jnp.where(is_valid, where_from, 0)
    token_index = assign // 2
    send_x = jnp.where(is_valid[:, None], tokens[token_index], jnp.zeros((), tokens.dtype))
    send_dy = jnp.where(is_valid[:, None], cotangent[token_index], jnp.zeros((), cotangent.dtype))
    send_gate = jnp.where(is_valid, gate_values.reshape(-1)[assign], 0.0)
    gate_high, gate_low = split_bf16(send_gate)
    lane = jnp.arange(EXTRA, dtype=jnp.int32)[None, :]
    extra = jnp.where(
        lane == 0, gate_high[:, None], jnp.where(lane == 1, gate_low[:, None], jnp.zeros((), jnp.bfloat16))
    )
    send = jnp.concatenate([send_x, send_dy, extra], axis=1)
    row_width = send.shape[1]
    arrived = lax.all_to_all(
        send.reshape(experts, capacity * row_width // LANES, LANES),
        "epc",
        split_axis=0,
        concat_axis=0,
        tiled=True,
    ).reshape(experts * capacity, row_width)
    swap = [(0, 1), (1, 0)]
    partner_rows = lax.ppermute(arrived, "core", swap)
    rows = jnp.concatenate([arrived, partner_rows], axis=0)
    rows_gate = rows[:, 2 * width].astype(jnp.float32) + rows[:, 2 * width + 1].astype(jnp.float32)
    token_part, gate_part, down_sum = expert_terms(
        rows[:, :width], rows[:, width : 2 * width], rows_gate, up_weight, down_weight
    )
    own = experts * capacity
    part_high, part_low = split_bf16(gate_part[own:])
    back_lane = jnp.arange(EXTRA, dtype=jnp.int32)[None, :]
    back_extra = jnp.where(
        back_lane == 0,
        part_high[:, None],
        jnp.where(back_lane == 1, part_low[:, None], jnp.zeros((), jnp.bfloat16)),
    )
    partner_back = lax.ppermute(
        jnp.concatenate([token_part[own:], back_extra], axis=1), "core", swap
    )
    token_sum = (
        token_part[:own].astype(jnp.float32) + partner_back[:, :width].astype(jnp.float32)
    ).astype(jnp.bfloat16)
    gate_sum = gate_part[:own] + (
        partner_back[:, width].astype(jnp.float32) + partner_back[:, width + 1].astype(jnp.float32)
    )
    sum_high, sum_low = split_bf16(gate_sum)
    ret_extra = jnp.where(
        back_lane == 0,
        sum_high[:, None],
        jnp.where(back_lane == 1, sum_low[:, None], jnp.zeros((), jnp.bfloat16)),
    )
    back = jnp.concatenate([token_sum, ret_extra], axis=1)
    back_width = back.shape[1]
    returned = lax.all_to_all(
        back.reshape(experts, capacity * back_width // LANES, LANES),
        "epc",
        split_axis=0,
        concat_axis=0,
        tiled=True,
    ).reshape(experts * capacity, back_width)
    picked = returned[position].astype(jnp.float32)
    token_grad = jnp.sum(picked[:, :width].reshape(tok_rows, 2, width), axis=1).astype(jnp.bfloat16)
    gate_grad = (picked[:, width] + picked[:, width + 1]).reshape(tok_rows, 2)
    return (token_grad, gate_grad, down_sum)


def solution(mesh):
    ep_size = mesh.shape["ep"]
    split_mesh = Mesh(
        mesh.devices.reshape(ep_size // 2, 2, mesh.shape["rep"]), ("epc", "core", "rep")
    )
    ep = ("epc", "core")
    return jax.shard_map(
        local,
        mesh=split_mesh,
        in_specs=(
            P(ep + ("rep",), None),
            P(ep + ("rep",), None),
            P(ep + ("rep",), None),
            P(ep + ("rep",), None),
            P("rep", ep),
            P(ep, "rep"),
        ),
        out_specs=(P(ep + ("rep",), None), P(ep + ("rep",), None), P(ep, "rep")),
        check_vma=False,
    )
```

```python
import math

import jax
import jax.numpy as jnp
from jax import lax
from jax.sharding import Mesh
from jax.sharding import PartitionSpec as P

tanh_scale = math.sqrt(2.0 / math.pi)
cubic_coef = 0.044715
EXTRA = 128
LANES = 128


def gelu_tanh(argument):
    inner_arg = tanh_scale * (argument + cubic_coef * argument * argument * argument)
    return 0.5 * argument * (1.0 + jnp.tanh(inner_arg))


def gelu_slope(argument):
    tanh_value = jnp.tanh(tanh_scale * (argument + cubic_coef * argument * argument * argument))
    return 0.5 * (1.0 + tanh_value) + 0.5 * argument * (
        1.0 - tanh_value * tanh_value
    ) * tanh_scale * (1.0 + 3.0 * cubic_coef * argument * argument)


def split_bf16(value):
    high = value.astype(jnp.bfloat16)
    low = (value - high.astype(jnp.float32)).astype(jnp.bfloat16)
    return high, low


def expert_terms(rows_x, rows_dy, rows_gate, up_full, down_full_t):
    contract_last = (((1,), (1,)), ((), ()))
    pre_act = jnp.dot(rows_x, up_full, preferred_element_type=jnp.float32)
    grad_hidden = jnp.dot(rows_dy, down_full_t, preferred_element_type=jnp.float32)
    hidden = gelu_tanh(pre_act)
    hidden_bf = hidden.astype(jnp.bfloat16)
    gate_part = jnp.sum(hidden * grad_hidden, axis=1)
    scaled_dy = (rows_gate[:, None] * rows_dy.astype(jnp.float32)).astype(jnp.bfloat16)
    down_term = lax.dot_general(
        hidden_bf, scaled_dy, (((0,), (0,)), ((), ())), preferred_element_type=jnp.float32
    )
    grad_pre = (rows_gate[:, None] * grad_hidden * gelu_slope(pre_act)).astype(jnp.bfloat16)
    token_part = lax.dot_general(
        grad_pre, up_full, contract_last, preferred_element_type=jnp.float32
    ).astype(jnp.bfloat16)
    return (token_part, gate_part, down_term)


def gate_lanes(value):
    high, low = split_bf16(value)
    lane = jnp.arange(EXTRA, dtype=jnp.int32)[None, :]
    return jnp.where(
        lane == 0, high[:, None], jnp.where(lane == 1, low[:, None], jnp.zeros((), jnp.bfloat16))
    )


def exchange(rows, experts):
    row_count, row_width = rows.shape
    return lax.all_to_all(
        rows.reshape(experts, row_count * row_width // (experts * LANES), LANES),
        "epc",
        split_axis=0,
        concat_axis=0,
        tiled=True,
    ).reshape(row_count, row_width)


def chunk_terms(arrived, width, up_full, down_full_t):
    swap = [(0, 1), (1, 0)]
    own = arrived.shape[0]
    rows = jnp.concatenate([arrived, lax.ppermute(arrived, "core", swap)], axis=0)
    rows_gate = rows[:, 2 * width].astype(jnp.float32) + rows[:, 2 * width + 1].astype(jnp.float32)
    token_part, gate_part, down_term = expert_terms(
        rows[:, :width], rows[:, width : 2 * width], rows_gate, up_full, down_full_t
    )
    partner_back = lax.ppermute(
        jnp.concatenate([token_part[own:], gate_lanes(gate_part[own:])], axis=1), "core", swap
    )
    token_sum = (
        token_part[:own].astype(jnp.float32) + partner_back[:, :width].astype(jnp.float32)
    ).astype(jnp.bfloat16)
    gate_sum = gate_part[:own] + (
        partner_back[:, width].astype(jnp.float32) + partner_back[:, width + 1].astype(jnp.float32)
    )
    return jnp.concatenate([token_sum, gate_lanes(gate_sum)], axis=1), down_term


def local(tokens, cotangent, expert_ids, gate_values, up_weight, down_weight):
    experts = lax.axis_size("epc")
    tok_rows, width = tokens.shape
    capacity = 5 * tok_rows // (2 * experts)
    assignments = 2 * tok_rows
    flat_ids = expert_ids.reshape(-1)
    onehot = (flat_ids[:, None] == jnp.arange(experts, dtype=jnp.int32)[None, :]).astype(jnp.int32)
    running_rank = jnp.cumsum(onehot, axis=0)
    slot_index = jnp.sum(onehot * running_rank, axis=1) - 1
    position = flat_ids * capacity + slot_index
    where_from = (
        jnp.full((experts * capacity,), -1, jnp.int32)
        .at[position]
        .set(jnp.arange(assignments, dtype=jnp.int32))
    )
    is_valid = where_from >= 0
    assign = jnp.where(is_valid, where_from, 0)
    token_index = assign // 2
    send_x = jnp.where(is_valid[:, None], tokens[token_index], jnp.zeros((), tokens.dtype))
    send_dy = jnp.where(is_valid[:, None], cotangent[token_index], jnp.zeros((), cotangent.dtype))
    send_gate = jnp.where(is_valid, gate_values.reshape(-1)[assign], 0.0)
    send = jnp.concatenate([send_x, send_dy, gate_lanes(send_gate)], axis=1).reshape(
        experts, capacity, -1
    )
    both_full = lax.all_gather(
        jnp.stack([up_weight, down_weight.T]), "rep", axis=1, tiled=True
    )
    split = (capacity + 1) // 2
    first_send = send[:, :split].reshape(experts * split, -1)
    second_send = send[:, split:].reshape(experts * (capacity - split), -1)
    first_arrived = exchange(first_send, experts)
    first_arrived, second_send = lax.optimization_barrier((first_arrived, second_send))
    second_arrived = exchange(second_send, experts)
    first_back, first_down = chunk_terms(first_arrived, width, both_full[0], both_full[1])
    first_returned = exchange(first_back, experts)
    second_back, second_down = chunk_terms(second_arrived, width, both_full[0], both_full[1])
    second_returned = exchange(second_back, experts)
    down_term = (first_down + second_down).astype(jnp.bfloat16)
    down_sum = (
        lax.psum_scatter(down_term, "rep", scatter_dimension=1, tiled=True)
        .astype(jnp.float32)
        .astype(jnp.bfloat16)
    )
    returned = jnp.concatenate(
        [
            first_returned.reshape(experts, split, -1),
            second_returned.reshape(experts, capacity - split, -1),
        ],
        axis=1,
    ).reshape(experts * capacity, -1)
    picked = returned[position].astype(jnp.float32)
    token_grad = jnp.sum(picked[:, :width].reshape(tok_rows, 2, width), axis=1).astype(jnp.bfloat16)
    gate_grad = (picked[:, width] + picked[:, width + 1]).reshape(tok_rows, 2)
    return (token_grad, gate_grad, down_sum)


def solution(mesh):
    ep_size = mesh.shape["ep"]
    split_mesh = Mesh(
        mesh.devices.reshape(ep_size // 2, 2, mesh.shape["rep"]), ("epc", "core", "rep")
    )
    ep = ("epc", "core")
    return jax.shard_map(
        local,
        mesh=split_mesh,
        in_specs=(
            P(ep + ("rep",), None),
            P(ep + ("rep",), None),
            P(ep + ("rep",), None),
            P(ep + ("rep",), None),
            P("rep", ep),
            P(ep, "rep"),
        ),
        out_specs=(P(ep + ("rep",), None), P(ep + ("rep",), None), P(ep, "rep")),
        check_vma=False,
    )
```

```python
import math

import jax
import jax.numpy as jnp
from jax import lax
from jax.sharding import Mesh
from jax.sharding import PartitionSpec as P

tanh_scale = math.sqrt(2.0 / math.pi)
cubic_coef = 0.044715
LANES = 128


def gelu_tanh(argument):
    inner_arg = tanh_scale * (argument + cubic_coef * argument * argument * argument)
    return 0.5 * argument * (1.0 + jnp.tanh(inner_arg))


def gelu_slope(argument):
    tanh_value = jnp.tanh(tanh_scale * (argument + cubic_coef * argument * argument * argument))
    return 0.5 * (1.0 + tanh_value) + 0.5 * argument * (
        1.0 - tanh_value * tanh_value
    ) * tanh_scale * (1.0 + 3.0 * cubic_coef * argument * argument)


def split_bf16(value):
    high = value.astype(jnp.bfloat16)
    low = (value - high.astype(jnp.float32)).astype(jnp.bfloat16)
    return high, low


def expert_terms(rows_x, rows_dy, rows_gate, up_weight, down_weight):
    contract_last = (((1,), (1,)), ((), ()))
    both_full = lax.all_gather(
        jnp.stack([up_weight, down_weight.T]), "rep", axis=1, tiled=True
    )
    up_full = both_full[0]
    pre_act = jnp.dot(rows_x, up_full, preferred_element_type=jnp.float32)
    grad_hidden = jnp.dot(rows_dy, both_full[1], preferred_element_type=jnp.float32)
    hidden = gelu_tanh(pre_act)
    hidden_bf = hidden.astype(jnp.bfloat16)
    gate_part = jnp.sum(hidden * grad_hidden, axis=1)
    scaled_dy = (rows_gate[:, None] * rows_dy.astype(jnp.float32)).astype(jnp.bfloat16)
    down_term = lax.dot_general(
        hidden_bf, scaled_dy, (((0,), (0,)), ((), ())), preferred_element_type=jnp.float32
    ).astype(jnp.bfloat16)
    down_sum = (
        lax.psum_scatter(down_term, "rep", scatter_dimension=1, tiled=True)
        .astype(jnp.float32)
        .astype(jnp.bfloat16)
    )
    grad_pre = (rows_gate[:, None] * grad_hidden * gelu_slope(pre_act)).astype(jnp.bfloat16)
    token_part = lax.dot_general(
        grad_pre, up_full, contract_last, preferred_element_type=jnp.float32
    ).astype(jnp.bfloat16)
    return (token_part, gate_part, down_sum)


def pack(rows, gate, experts):
    count, row_width = rows.shape
    per = count // experts
    high, low = split_bf16(gate)
    gate_row = jnp.concatenate(
        [
            high.reshape(experts, per),
            low.reshape(experts, per),
            jnp.zeros((experts, LANES - 2 * per), jnp.bfloat16),
        ],
        axis=1,
    )
    return jnp.concatenate(
        [rows.reshape(experts, per * row_width // LANES, LANES), gate_row[:, None, :]], axis=1
    )


def unpack(packed, per):
    experts = packed.shape[0]
    body = packed[:, :-1].reshape(experts * per, -1)
    gate_row = packed[:, -1].astype(jnp.float32)
    return body, (gate_row[:, :per] + gate_row[:, per : 2 * per]).reshape(-1)


def exchange(packed):
    return lax.all_to_all(packed, "epc", split_axis=0, concat_axis=0, tiled=True)


def local(tokens, cotangent, expert_ids, gate_values, up_weight, down_weight):
    experts = lax.axis_size("epc")
    tok_rows, width = tokens.shape
    capacity = 5 * tok_rows // (2 * experts)
    assignments = 2 * tok_rows
    flat_ids = expert_ids.reshape(-1)
    onehot = (flat_ids[:, None] == jnp.arange(experts, dtype=jnp.int32)[None, :]).astype(jnp.int32)
    running_rank = jnp.cumsum(onehot, axis=0)
    slot_index = jnp.sum(onehot * running_rank, axis=1) - 1
    position = flat_ids * capacity + slot_index
    where_from = (
        jnp.full((experts * capacity,), -1, jnp.int32)
        .at[position]
        .set(jnp.arange(assignments, dtype=jnp.int32))
    )
    is_valid = where_from >= 0
    assign = jnp.where(is_valid, where_from, 0)
    token_index = assign // 2
    send_x = jnp.where(is_valid[:, None], tokens[token_index], jnp.zeros((), tokens.dtype))
    send_dy = jnp.where(is_valid[:, None], cotangent[token_index], jnp.zeros((), cotangent.dtype))
    send_gate = jnp.where(is_valid, gate_values.reshape(-1)[assign], 0.0)
    arrived = exchange(pack(jnp.concatenate([send_x, send_dy], axis=1), send_gate, experts))
    swap = [(0, 1), (1, 0)]
    own_rows, own_gate = unpack(arrived, capacity)
    partner_rows, partner_gate = unpack(lax.ppermute(arrived, "core", swap), capacity)
    rows = jnp.concatenate([own_rows, partner_rows], axis=0)
    rows_gate = jnp.concatenate([own_gate, partner_gate], axis=0)
    token_part, gate_part, down_sum = expert_terms(
        rows[:, :width], rows[:, width:], rows_gate, up_weight, down_weight
    )
    own = experts * capacity
    partner_token, partner_part = unpack(
        lax.ppermute(pack(token_part[own:], gate_part[own:], experts), "core", swap), capacity
    )
    token_sum = (
        token_part[:own].astype(jnp.float32) + partner_token.astype(jnp.float32)
    ).astype(jnp.bfloat16)
    gate_sum = gate_part[:own] + partner_part
    returned, returned_gate = unpack(exchange(pack(token_sum, gate_sum, experts)), capacity)
    pair = position.reshape(tok_rows, 2)
    token_grad = (
        returned[pair[:, 0]].astype(jnp.float32) + returned[pair[:, 1]].astype(jnp.float32)
    ).astype(jnp.bfloat16)
    gate_grad = returned_gate[position].reshape(tok_rows, 2)
    return (token_grad, gate_grad, down_sum)


def solution(mesh):
    ep_size = mesh.shape["ep"]
    split_mesh = Mesh(
        mesh.devices.reshape(ep_size // 2, 2, mesh.shape["rep"]), ("epc", "core", "rep")
    )
    ep = ("epc", "core")
    return jax.shard_map(
        local,
        mesh=split_mesh,
        in_specs=(
            P(ep + ("rep",), None),
            P(ep + ("rep",), None),
            P(ep + ("rep",), None),
            P(ep + ("rep",), None),
            P("rep", ep),
            P(ep, "rep"),
        ),
        out_specs=(P(ep + ("rep",), None), P(ep + ("rep",), None), P(ep, "rep")),
        check_vma=False,
    )
```

```python
import math

import jax
import jax.numpy as jnp
from jax import lax
from jax.sharding import Mesh
from jax.sharding import PartitionSpec as P

tanh_scale = math.sqrt(2.0 / math.pi)
cubic_coef = 0.044715
LANES = 128


def gelu_tanh(argument):
    inner_arg = tanh_scale * (argument + cubic_coef * argument * argument * argument)
    return 0.5 * argument * (1.0 + jnp.tanh(inner_arg))


def gelu_slope(argument):
    tanh_value = jnp.tanh(tanh_scale * (argument + cubic_coef * argument * argument * argument))
    return 0.5 * (1.0 + tanh_value) + 0.5 * argument * (
        1.0 - tanh_value * tanh_value
    ) * tanh_scale * (1.0 + 3.0 * cubic_coef * argument * argument)


def split_bf16(value):
    high = value.astype(jnp.bfloat16)
    low = (value - high.astype(jnp.float32)).astype(jnp.bfloat16)
    return high, low


def expert_terms(rows_x, rows_dy, rows_gate, up_weight, down_weight):
    contract_last = (((1,), (1,)), ((), ()))
    both_full = lax.all_gather(
        jnp.stack([up_weight, down_weight.T]), "rep", axis=1, tiled=True
    )
    up_full = both_full[0]
    pre_act = jnp.dot(rows_x, up_full, preferred_element_type=jnp.float32)
    grad_hidden = jnp.dot(rows_dy, both_full[1], preferred_element_type=jnp.float32)
    hidden = gelu_tanh(pre_act)
    hidden_bf = hidden.astype(jnp.bfloat16)
    gate_part = jnp.sum(hidden * grad_hidden, axis=1)
    scaled_dy = (rows_gate[:, None] * rows_dy.astype(jnp.float32)).astype(jnp.bfloat16)
    down_term = lax.dot_general(
        hidden_bf, scaled_dy, (((0,), (0,)), ((), ())), preferred_element_type=jnp.float32
    ).astype(jnp.bfloat16)
    down_sum = (
        lax.psum_scatter(down_term, "rep", scatter_dimension=1, tiled=True)
        .astype(jnp.float32)
        .astype(jnp.bfloat16)
    )
    grad_pre = (rows_gate[:, None] * grad_hidden * gelu_slope(pre_act)).astype(jnp.bfloat16)
    token_part = lax.dot_general(
        grad_pre, up_full, contract_last, preferred_element_type=jnp.float32
    ).astype(jnp.bfloat16)
    return (token_part, gate_part, down_sum)


def exchange(packed):
    return lax.all_to_all(packed, "epc", split_axis=0, concat_axis=0, tiled=True)


def local(tokens, cotangent, expert_ids, gate_values, up_weight, down_weight):
    experts = lax.axis_size("epc")
    tok_rows, width = tokens.shape
    capacity = 5 * tok_rows // (2 * experts)
    assignments = 2 * tok_rows
    flat_ids = expert_ids.reshape(-1)
    onehot = (flat_ids[:, None] == jnp.arange(experts, dtype=jnp.int32)[None, :]).astype(jnp.int32)
    running_rank = jnp.cumsum(onehot, axis=0)
    slot_index = jnp.sum(onehot * running_rank, axis=1) - 1
    position = flat_ids * capacity + slot_index
    where_from = (
        jnp.full((experts * capacity,), -1, jnp.int32)
        .at[position]
        .set(jnp.arange(assignments, dtype=jnp.int32))
    )
    is_valid = where_from >= 0
    assign = jnp.where(is_valid, where_from, 0)
    token_index = assign // 2
    send_x = jnp.where(is_valid[:, None], tokens[token_index], jnp.zeros((), tokens.dtype))
    send_dy = jnp.where(is_valid[:, None], cotangent[token_index], jnp.zeros((), cotangent.dtype))
    send_gate = jnp.where(is_valid, gate_values.reshape(-1)[assign], 0.0)
    pair_rows = jnp.concatenate([send_x, send_dy], axis=1)
    arrived = exchange(pair_rows.reshape(experts, -1, LANES))
    here = lax.axis_index("epc")
    arrived_gate = lax.dynamic_slice_in_dim(
        lax.all_gather(send_gate, "epc", axis=0, tiled=False), here * capacity, capacity, axis=1
    ).reshape(-1)
    arrived, arrived_gate = lax.optimization_barrier((arrived, arrived_gate))
    swap = [(0, 1), (1, 0)]
    rows = jnp.concatenate(
        [arrived, lax.ppermute(arrived, "core", swap)], axis=0
    ).reshape(2 * experts * capacity, 2 * width)
    rows_gate = jnp.concatenate([arrived_gate, lax.ppermute(arrived_gate, "core", swap)], axis=0)
    token_part, gate_part, down_sum = expert_terms(
        rows[:, :width], rows[:, width:], rows_gate, up_weight, down_weight
    )
    own = experts * capacity
    partner_token = lax.ppermute(token_part[own:], "core", swap)
    partner_part = lax.ppermute(gate_part[own:], "core", swap)
    token_sum = (
        token_part[:own].astype(jnp.float32) + partner_token.astype(jnp.float32)
    ).astype(jnp.bfloat16)
    gate_sum = gate_part[:own] + partner_part
    returned = exchange(token_sum.reshape(experts, -1, LANES)).reshape(experts * capacity, width)
    returned_gate = lax.dynamic_slice_in_dim(
        lax.all_gather(gate_sum, "epc", axis=0, tiled=False), here * capacity, capacity, axis=1
    ).reshape(-1)
    pair = position.reshape(tok_rows, 2)
    token_grad = (
        returned[pair[:, 0]].astype(jnp.float32) + returned[pair[:, 1]].astype(jnp.float32)
    ).astype(jnp.bfloat16)
    gate_grad = returned_gate[position].reshape(tok_rows, 2)
    return (token_grad, gate_grad, down_sum)


def solution(mesh):
    ep_size = mesh.shape["ep"]
    split_mesh = Mesh(
        mesh.devices.reshape(ep_size // 2, 2, mesh.shape["rep"]), ("epc", "core", "rep")
    )
    ep = ("epc", "core")
    return jax.shard_map(
        local,
        mesh=split_mesh,
        in_specs=(
            P(ep + ("rep",), None),
            P(ep + ("rep",), None),
            P(ep + ("rep",), None),
            P(ep + ("rep",), None),
            P("rep", ep),
            P(ep, "rep"),
        ),
        out_specs=(P(ep + ("rep",), None), P(ep + ("rep",), None), P(ep, "rep")),
        check_vma=False,
    )
```

```python
import math

import jax
import jax.numpy as jnp
from jax import lax
from jax.sharding import Mesh
from jax.sharding import PartitionSpec as P

tanh_scale = math.sqrt(2.0 / math.pi)
cubic_coef = 0.044715
EXTRA = 128
LANES = 128


def gelu_tanh(argument):
    inner_arg = tanh_scale * (argument + cubic_coef * argument * argument * argument)
    return 0.5 * argument * (1.0 + jnp.tanh(inner_arg))


def gelu_slope(argument):
    tanh_value = jnp.tanh(tanh_scale * (argument + cubic_coef * argument * argument * argument))
    return 0.5 * (1.0 + tanh_value) + 0.5 * argument * (
        1.0 - tanh_value * tanh_value
    ) * tanh_scale * (1.0 + 3.0 * cubic_coef * argument * argument)


def split_bf16(value):
    high = value.astype(jnp.bfloat16)
    low = (value - high.astype(jnp.float32)).astype(jnp.bfloat16)
    return high, low


def expert_terms(rows_x, rows_scaled, up_weight, down_weight):
    contract_last = (((1,), (1,)), ((), ()))
    both_full = lax.all_gather(
        jnp.stack([up_weight, down_weight.T]), "rep", axis=1, tiled=True
    )
    up_full = both_full[0]
    pre_act = jnp.dot(rows_x, up_full, preferred_element_type=jnp.float32)
    gated_grad_hidden = jnp.dot(rows_scaled, both_full[1], preferred_element_type=jnp.float32)
    hidden = gelu_tanh(pre_act)
    hidden_bf = hidden.astype(jnp.bfloat16)
    gated_part = jnp.sum(hidden * gated_grad_hidden, axis=1)
    down_term = lax.dot_general(
        hidden_bf, rows_scaled, (((0,), (0,)), ((), ())), preferred_element_type=jnp.float32
    ).astype(jnp.bfloat16)
    down_sum = (
        lax.psum_scatter(down_term, "rep", scatter_dimension=1, tiled=True)
        .astype(jnp.float32)
        .astype(jnp.bfloat16)
    )
    grad_pre = (gated_grad_hidden * gelu_slope(pre_act)).astype(jnp.bfloat16)
    token_part = lax.dot_general(
        grad_pre, up_full, contract_last, preferred_element_type=jnp.float32
    ).astype(jnp.bfloat16)
    return (token_part, gated_part, down_sum)


def local(tokens, cotangent, expert_ids, gate_values, up_weight, down_weight):
    experts = lax.axis_size("epc")
    tok_rows, width = tokens.shape
    capacity = 5 * tok_rows // (2 * experts)
    assignments = 2 * tok_rows
    flat_ids = expert_ids.reshape(-1)
    onehot = (flat_ids[:, None] == jnp.arange(experts, dtype=jnp.int32)[None, :]).astype(jnp.int32)
    running_rank = jnp.cumsum(onehot, axis=0)
    slot_index = jnp.sum(onehot * running_rank, axis=1) - 1
    position = flat_ids * capacity + slot_index
    where_from = (
        jnp.full((experts * capacity,), -1, jnp.int32)
        .at[position]
        .set(jnp.arange(assignments, dtype=jnp.int32))
    )
    is_valid = where_from >= 0
    assign = jnp.where(is_valid, where_from, 0)
    token_index = assign // 2
    send_x = jnp.where(is_valid[:, None], tokens[token_index], jnp.zeros((), tokens.dtype))
    send_gate = jnp.where(is_valid, gate_values.reshape(-1)[assign], 0.0)
    send_scaled = (send_gate[:, None] * cotangent[token_index].astype(jnp.float32)).astype(
        jnp.bfloat16
    )
    send = jnp.concatenate([send_x, send_scaled], axis=1)
    row_width = send.shape[1]
    arrived = lax.all_to_all(
        send.reshape(experts, capacity * row_width // LANES, LANES),
        "epc",
        split_axis=0,
        concat_axis=0,
        tiled=True,
    ).reshape(experts * capacity, row_width)
    swap = [(0, 1), (1, 0)]
    partner_rows = lax.ppermute(arrived, "core", swap)
    rows = jnp.concatenate([arrived, partner_rows], axis=0)
    token_part, gate_part, down_sum = expert_terms(
        rows[:, :width], rows[:, width:], up_weight, down_weight
    )
    own = experts * capacity
    part_high, part_low = split_bf16(gate_part[own:])
    back_lane = jnp.arange(EXTRA, dtype=jnp.int32)[None, :]
    back_extra = jnp.where(
        back_lane == 0,
        part_high[:, None],
        jnp.where(back_lane == 1, part_low[:, None], jnp.zeros((), jnp.bfloat16)),
    )
    partner_back = lax.ppermute(
        jnp.concatenate([token_part[own:], back_extra], axis=1), "core", swap
    )
    token_sum = (
        token_part[:own].astype(jnp.float32) + partner_back[:, :width].astype(jnp.float32)
    ).astype(jnp.bfloat16)
    gate_sum = gate_part[:own] + (
        partner_back[:, width].astype(jnp.float32) + partner_back[:, width + 1].astype(jnp.float32)
    )
    sum_high, sum_low = split_bf16(gate_sum)
    ret_extra = jnp.where(
        back_lane == 0,
        sum_high[:, None],
        jnp.where(back_lane == 1, sum_low[:, None], jnp.zeros((), jnp.bfloat16)),
    )
    back = jnp.concatenate([token_sum, ret_extra], axis=1)
    back_width = back.shape[1]
    returned = lax.all_to_all(
        back.reshape(experts, capacity * back_width // LANES, LANES),
        "epc",
        split_axis=0,
        concat_axis=0,
        tiled=True,
    ).reshape(experts * capacity, back_width)
    picked = returned[position].astype(jnp.float32)
    token_grad = jnp.sum(picked[:, :width].reshape(tok_rows, 2, width), axis=1).astype(jnp.bfloat16)
    gated_grad = picked[:, width] + picked[:, width + 1]
    gate_grad = (gated_grad / gate_values.reshape(-1)).reshape(tok_rows, 2)
    return (token_grad, gate_grad, down_sum)


def solution(mesh):
    ep_size = mesh.shape["ep"]
    split_mesh = Mesh(
        mesh.devices.reshape(ep_size // 2, 2, mesh.shape["rep"]), ("epc", "core", "rep")
    )
    ep = ("epc", "core")
    return jax.shard_map(
        local,
        mesh=split_mesh,
        in_specs=(
            P(ep + ("rep",), None),
            P(ep + ("rep",), None),
            P(ep + ("rep",), None),
            P(ep + ("rep",), None),
            P("rep", ep),
            P(ep, "rep"),
        ),
        out_specs=(P(ep + ("rep",), None), P(ep + ("rep",), None), P(ep, "rep")),
        check_vma=False,
    )
```

```python
import math

import jax
import jax.numpy as jnp
from jax import lax
from jax.sharding import Mesh
from jax.sharding import PartitionSpec as P

tanh_scale = math.sqrt(2.0 / math.pi)
cubic_coef = 0.044715
EXTRA = 128
LANES = 128


def gelu_tanh(argument):
    inner_arg = tanh_scale * (argument + cubic_coef * argument * argument * argument)
    return 0.5 * argument * (1.0 + jnp.tanh(inner_arg))


def gelu_slope(argument):
    tanh_value = jnp.tanh(tanh_scale * (argument + cubic_coef * argument * argument * argument))
    return 0.5 * (1.0 + tanh_value) + 0.5 * argument * (
        1.0 - tanh_value * tanh_value
    ) * tanh_scale * (1.0 + 3.0 * cubic_coef * argument * argument)


def split_bf16(value):
    high = value.astype(jnp.bfloat16)
    low = (value - high.astype(jnp.float32)).astype(jnp.bfloat16)
    return high, low


def expert_terms(rows_x, rows_scaled, up_weight, down_weight):
    contract_last = (((1,), (1,)), ((), ()))
    both_full = lax.all_gather(
        jnp.stack([up_weight, down_weight.T]), "rep", axis=1, tiled=True
    )
    up_full = both_full[0]
    pre_act = jnp.dot(rows_x, up_full, preferred_element_type=jnp.float32)
    gated_grad_hidden = jnp.dot(rows_scaled, both_full[1], preferred_element_type=jnp.float32)
    hidden = gelu_tanh(pre_act)
    hidden_bf = hidden.astype(jnp.bfloat16)
    gated_part = jnp.sum(hidden * gated_grad_hidden, axis=1)
    down_term = lax.dot_general(
        hidden_bf, rows_scaled, (((0,), (0,)), ((), ())), preferred_element_type=jnp.float32
    ).astype(jnp.bfloat16)
    down_sum = (
        lax.psum_scatter(down_term, "rep", scatter_dimension=1, tiled=True)
        .astype(jnp.float32)
        .astype(jnp.bfloat16)
    )
    grad_pre = (gated_grad_hidden * gelu_slope(pre_act)).astype(jnp.bfloat16)
    token_part = lax.dot_general(
        grad_pre, up_full, contract_last, preferred_element_type=jnp.float32
    ).astype(jnp.bfloat16)
    return (token_part, gated_part, down_sum)


def local(tokens, cotangent, expert_ids, gate_values, up_weight, down_weight):
    experts = lax.axis_size("epc")
    tok_rows, width = tokens.shape
    capacity = 5 * tok_rows // (2 * experts)
    assignments = 2 * tok_rows
    flat_ids = expert_ids.reshape(-1)
    onehot = (flat_ids[:, None] == jnp.arange(experts, dtype=jnp.int32)[None, :]).astype(jnp.int32)
    running_rank = jnp.cumsum(onehot, axis=0)
    slot_index = jnp.sum(onehot * running_rank, axis=1) - 1
    position = flat_ids * capacity + slot_index
    where_from = (
        jnp.full((experts * capacity,), -1, jnp.int32)
        .at[position]
        .set(jnp.arange(assignments, dtype=jnp.int32))
    )
    is_valid = where_from >= 0
    assign = jnp.where(is_valid, where_from, 0)
    token_index = assign // 2
    send_x = jnp.where(is_valid[:, None], tokens[token_index], jnp.zeros((), tokens.dtype))
    send_gate = jnp.where(is_valid, gate_values.reshape(-1)[assign], 0.0)
    send_scaled = (send_gate[:, None] * cotangent[token_index].astype(jnp.float32)).astype(
        jnp.bfloat16
    )
    send = jnp.concatenate([send_x, send_scaled], axis=1)
    row_width = send.shape[1]
    arrived = lax.all_to_all(
        send.reshape(experts, capacity * row_width // LANES, LANES),
        "epc",
        split_axis=0,
        concat_axis=0,
        tiled=True,
    ).reshape(experts * capacity, row_width)
    swap = [(0, 1), (1, 0)]
    partner_rows = lax.ppermute(arrived, "core", swap)
    rows = jnp.concatenate([arrived, partner_rows], axis=0)
    token_part, gate_part, down_sum = expert_terms(
        rows[:, :width], rows[:, width:], up_weight, down_weight
    )
    own = experts * capacity
    part_high, part_low = split_bf16(gate_part[own:])
    back_lane = jnp.arange(EXTRA, dtype=jnp.int32)[None, :]
    back_extra = jnp.where(
        back_lane == 0,
        part_high[:, None],
        jnp.where(back_lane == 1, part_low[:, None], jnp.zeros((), jnp.bfloat16)),
    )
    partner_back = lax.ppermute(
        jnp.concatenate([token_part[own:], back_extra], axis=1), "core", swap
    )
    token_sum = (
        token_part[:own].astype(jnp.float32) + partner_back[:, :width].astype(jnp.float32)
    ).astype(jnp.bfloat16)
    gate_sum = gate_part[:own] + (
        partner_back[:, width].astype(jnp.float32) + partner_back[:, width + 1].astype(jnp.float32)
    )
    sum_high, sum_low = split_bf16(gate_sum)
    ret_extra = jnp.where(
        back_lane == 0,
        sum_high[:, None],
        jnp.where(back_lane == 1, sum_low[:, None], jnp.zeros((), jnp.bfloat16)),
    )
    back = jnp.concatenate([token_sum, ret_extra], axis=1)
    back_width = back.shape[1]
    returned = lax.all_to_all(
        back.reshape(experts, capacity * back_width // LANES, LANES),
        "epc",
        split_axis=0,
        concat_axis=0,
        tiled=True,
    ).reshape(experts * capacity, back_width)
    slots = jnp.arange(experts * capacity, dtype=jnp.int32)[None, None, :]
    select = jnp.any(position.reshape(tok_rows, 2)[:, :, None] == slots, axis=1)
    token_grad = jnp.dot(
        select.astype(jnp.bfloat16), returned[:, :width], preferred_element_type=jnp.float32
    ).astype(jnp.bfloat16)
    returned_gate = returned[:, width].astype(jnp.float32) + returned[:, width + 1].astype(
        jnp.float32
    )
    gated_grad = returned_gate[position]
    gate_grad = (gated_grad / gate_values.reshape(-1)).reshape(tok_rows, 2)
    return (token_grad, gate_grad, down_sum)


def solution(mesh):
    ep_size = mesh.shape["ep"]
    split_mesh = Mesh(
        mesh.devices.reshape(ep_size // 2, 2, mesh.shape["rep"]), ("epc", "core", "rep")
    )
    ep = ("epc", "core")
    return jax.shard_map(
        local,
        mesh=split_mesh,
        in_specs=(
            P(ep + ("rep",), None),
            P(ep + ("rep",), None),
            P(ep + ("rep",), None),
            P(ep + ("rep",), None),
            P("rep", ep),
            P(ep, "rep"),
        ),
        out_specs=(P(ep + ("rep",), None), P(ep + ("rep",), None), P(ep, "rep")),
        check_vma=False,
    )
```

```python
import math

import jax
import jax.numpy as jnp
from jax import lax
from jax.sharding import Mesh
from jax.sharding import PartitionSpec as P

tanh_scale = math.sqrt(2.0 / math.pi)
cubic_coef = 0.044715
EXTRA = 128
LANES = 128


def gelu_tanh(argument):
    inner_arg = tanh_scale * (argument + cubic_coef * argument * argument * argument)
    return 0.5 * argument * (1.0 + jnp.tanh(inner_arg))


def gelu_slope(argument):
    tanh_value = jnp.tanh(tanh_scale * (argument + cubic_coef * argument * argument * argument))
    return 0.5 * (1.0 + tanh_value) + 0.5 * argument * (
        1.0 - tanh_value * tanh_value
    ) * tanh_scale * (1.0 + 3.0 * cubic_coef * argument * argument)


def split_bf16(value):
    high = value.astype(jnp.bfloat16)
    low = (value - high.astype(jnp.float32)).astype(jnp.bfloat16)
    return high, low


def expert_terms(rows_x, rows_scaled, up_full, down_full_t):
    contract_last = (((1,), (1,)), ((), ()))
    pre_act = jnp.dot(rows_x, up_full, preferred_element_type=jnp.float32)
    gated_grad_hidden = jnp.dot(rows_scaled, down_full_t, preferred_element_type=jnp.float32)
    hidden = gelu_tanh(pre_act)
    hidden_bf = hidden.astype(jnp.bfloat16)
    gated_part = jnp.sum(hidden * gated_grad_hidden, axis=1)
    down_term = lax.dot_general(
        hidden_bf, rows_scaled, (((0,), (0,)), ((), ())), preferred_element_type=jnp.float32
    )
    grad_pre = (gated_grad_hidden * gelu_slope(pre_act)).astype(jnp.bfloat16)
    token_part = lax.dot_general(
        grad_pre, up_full, contract_last, preferred_element_type=jnp.float32
    ).astype(jnp.bfloat16)
    return (token_part, gated_part, down_term)


def local(tokens, cotangent, expert_ids, gate_values, up_weight, down_weight):
    experts = lax.axis_size("epc")
    tok_rows, width = tokens.shape
    capacity = 5 * tok_rows // (2 * experts)
    assignments = 2 * tok_rows
    flat_ids = expert_ids.reshape(-1)
    onehot = (flat_ids[:, None] == jnp.arange(experts, dtype=jnp.int32)[None, :]).astype(jnp.int32)
    running_rank = jnp.cumsum(onehot, axis=0)
    slot_index = jnp.sum(onehot * running_rank, axis=1) - 1
    position = flat_ids * capacity + slot_index
    where_from = (
        jnp.full((experts * capacity,), -1, jnp.int32)
        .at[position]
        .set(jnp.arange(assignments, dtype=jnp.int32))
    )
    is_valid = where_from >= 0
    assign = jnp.where(is_valid, where_from, 0)
    token_index = assign // 2
    send_x = jnp.where(is_valid[:, None], tokens[token_index], jnp.zeros((), tokens.dtype))
    send_gate = jnp.where(is_valid, gate_values.reshape(-1)[assign], 0.0)
    send_scaled = (send_gate[:, None] * cotangent[token_index].astype(jnp.float32)).astype(
        jnp.bfloat16
    )
    send = jnp.concatenate([send_x, send_scaled], axis=1)
    row_width = send.shape[1]
    arrived = lax.all_to_all(
        send.reshape(experts, capacity * row_width // LANES, LANES),
        "epc",
        split_axis=0,
        concat_axis=0,
        tiled=True,
    ).reshape(experts * capacity, row_width)
    swap = [(0, 1), (1, 0)]
    partner_rows = lax.ppermute(arrived, "core", swap)
    both_full = lax.all_gather(
        jnp.stack([up_weight, down_weight.T]), "rep", axis=1, tiled=True
    )
    own_token, own_gate, own_down = expert_terms(
        arrived[:, :width], arrived[:, width:], both_full[0], both_full[1]
    )
    other_token, other_gate, other_down = expert_terms(
        partner_rows[:, :width], partner_rows[:, width:], both_full[0], both_full[1]
    )
    down_sum = (
        lax.psum_scatter((own_down + other_down).astype(jnp.bfloat16), "rep", scatter_dimension=1, tiled=True)
        .astype(jnp.float32)
        .astype(jnp.bfloat16)
    )
    part_high, part_low = split_bf16(other_gate)
    back_lane = jnp.arange(EXTRA, dtype=jnp.int32)[None, :]
    back_extra = jnp.where(
        back_lane == 0,
        part_high[:, None],
        jnp.where(back_lane == 1, part_low[:, None], jnp.zeros((), jnp.bfloat16)),
    )
    partner_back = lax.ppermute(
        jnp.concatenate([other_token, back_extra], axis=1), "core", swap
    )
    token_sum = (
        own_token.astype(jnp.float32) + partner_back[:, :width].astype(jnp.float32)
    ).astype(jnp.bfloat16)
    gate_sum = own_gate + (
        partner_back[:, width].astype(jnp.float32) + partner_back[:, width + 1].astype(jnp.float32)
    )
    sum_high, sum_low = split_bf16(gate_sum)
    ret_extra = jnp.where(
        back_lane == 0,
        sum_high[:, None],
        jnp.where(back_lane == 1, sum_low[:, None], jnp.zeros((), jnp.bfloat16)),
    )
    back = jnp.concatenate([token_sum, ret_extra], axis=1)
    back_width = back.shape[1]
    returned = lax.all_to_all(
        back.reshape(experts, capacity * back_width // LANES, LANES),
        "epc",
        split_axis=0,
        concat_axis=0,
        tiled=True,
    ).reshape(experts * capacity, back_width)
    slots = jnp.arange(experts * capacity, dtype=jnp.int32)[None, None, :]
    select = jnp.any(position.reshape(tok_rows, 2)[:, :, None] == slots, axis=1)
    token_grad = jnp.dot(
        select.astype(jnp.bfloat16), returned[:, :width], preferred_element_type=jnp.float32
    ).astype(jnp.bfloat16)
    returned_gate = returned[:, width].astype(jnp.float32) + returned[:, width + 1].astype(
        jnp.float32
    )
    gated_grad = returned_gate[position]
    gate_grad = (gated_grad / gate_values.reshape(-1)).reshape(tok_rows, 2)
    return (token_grad, gate_grad, down_sum)


def solution(mesh):
    ep_size = mesh.shape["ep"]
    split_mesh = Mesh(
        mesh.devices.reshape(ep_size // 2, 2, mesh.shape["rep"]), ("epc", "core", "rep")
    )
    ep = ("epc", "core")
    return jax.shard_map(
        local,
        mesh=split_mesh,
        in_specs=(
            P(ep + ("rep",), None),
            P(ep + ("rep",), None),
            P(ep + ("rep",), None),
            P(ep + ("rep",), None),
            P("rep", ep),
            P(ep, "rep"),
        ),
        out_specs=(P(ep + ("rep",), None), P(ep + ("rep",), None), P(ep, "rep")),
        check_vma=False,
    )
```

```python
import math

import jax
import jax.numpy as jnp
from jax import lax
from jax.sharding import Mesh
from jax.sharding import PartitionSpec as P

tanh_scale = math.sqrt(2.0 / math.pi)
cubic_coef = 0.044715
EXTRA = 128
LANES = 128


def gelu_tanh(argument):
    inner_arg = tanh_scale * (argument + cubic_coef * argument * argument * argument)
    return 0.5 * argument * (1.0 + jnp.tanh(inner_arg))


def gelu_slope(argument):
    tanh_value = jnp.tanh(tanh_scale * (argument + cubic_coef * argument * argument * argument))
    return 0.5 * (1.0 + tanh_value) + 0.5 * argument * (
        1.0 - tanh_value * tanh_value
    ) * tanh_scale * (1.0 + 3.0 * cubic_coef * argument * argument)


def split_bf16(value):
    high = value.astype(jnp.bfloat16)
    low = (value - high.astype(jnp.float32)).astype(jnp.bfloat16)
    return high, low


def expert_terms(rows_x, rows_scaled, up_weight, down_weight):
    contract_last = (((1,), (1,)), ((), ()))
    both_full = lax.all_gather(
        jnp.stack([up_weight, down_weight.T]), "rep", axis=1, tiled=True
    )
    up_full = both_full[0]
    pre_act = jnp.dot(rows_x, up_full, preferred_element_type=jnp.float32)
    gated_grad_hidden = jnp.dot(rows_scaled, both_full[1], preferred_element_type=jnp.float32)
    hidden = gelu_tanh(pre_act)
    hidden_bf = hidden.astype(jnp.bfloat16)
    gated_part = jnp.sum(hidden * gated_grad_hidden, axis=1)
    down_term = lax.dot_general(
        hidden_bf, rows_scaled, (((0,), (0,)), ((), ())), preferred_element_type=jnp.float32
    ).astype(jnp.bfloat16)
    down_sum = (
        lax.psum_scatter(down_term, "rep", scatter_dimension=1, tiled=True)
        .astype(jnp.float32)
        .astype(jnp.bfloat16)
    )
    grad_pre = (gated_grad_hidden * gelu_slope(pre_act)).astype(jnp.bfloat16)
    token_part = lax.dot_general(
        grad_pre, up_full, contract_last, preferred_element_type=jnp.float32
    ).astype(jnp.bfloat16)
    return (token_part, gated_part, down_sum)


def local(tokens, cotangent, expert_ids, gate_values, up_weight, down_weight):
    experts = lax.axis_size("epc")
    tok_rows, width = tokens.shape
    capacity = 5 * tok_rows // (2 * experts)
    assignments = 2 * tok_rows
    flat_ids = expert_ids.reshape(-1)
    onehot = (flat_ids[:, None] == jnp.arange(experts, dtype=jnp.int32)[None, :]).astype(jnp.int32)
    running_rank = jnp.cumsum(onehot, axis=0)
    slot_index = jnp.sum(onehot * running_rank, axis=1) - 1
    position = flat_ids * capacity + slot_index
    where_from = (
        jnp.full((experts * capacity,), -1, jnp.int32)
        .at[position]
        .set(jnp.arange(assignments, dtype=jnp.int32))
    )
    is_valid = where_from >= 0
    assign = jnp.where(is_valid, where_from, 0)
    token_index = assign // 2
    pick = (
        (token_index[:, None] == jnp.arange(tok_rows, dtype=jnp.int32)[None, :]) & is_valid[:, None]
    ).astype(jnp.bfloat16)
    send_x = jnp.dot(pick, tokens, preferred_element_type=jnp.float32).astype(jnp.bfloat16)
    send_gate = jnp.where(is_valid, gate_values.reshape(-1)[assign], 0.0)
    send_scaled = (
        send_gate[:, None] * jnp.dot(pick, cotangent, preferred_element_type=jnp.float32)
    ).astype(jnp.bfloat16)
    send = jnp.concatenate([send_x, send_scaled], axis=1)
    row_width = send.shape[1]
    arrived = lax.all_to_all(
        send.reshape(experts, capacity * row_width // LANES, LANES),
        "epc",
        split_axis=0,
        concat_axis=0,
        tiled=True,
    ).reshape(experts * capacity, row_width)
    swap = [(0, 1), (1, 0)]
    partner_rows = lax.ppermute(arrived, "core", swap)
    rows = jnp.concatenate([arrived, partner_rows], axis=0)
    token_part, gate_part, down_sum = expert_terms(
        rows[:, :width], rows[:, width:], up_weight, down_weight
    )
    own = experts * capacity
    part_high, part_low = split_bf16(gate_part[own:])
    back_lane = jnp.arange(EXTRA, dtype=jnp.int32)[None, :]
    back_extra = jnp.where(
        back_lane == 0,
        part_high[:, None],
        jnp.where(back_lane == 1, part_low[:, None], jnp.zeros((), jnp.bfloat16)),
    )
    partner_back = lax.ppermute(
        jnp.concatenate([token_part[own:], back_extra], axis=1), "core", swap
    )
    token_sum = (
        token_part[:own].astype(jnp.float32) + partner_back[:, :width].astype(jnp.float32)
    ).astype(jnp.bfloat16)
    gate_sum = gate_part[:own] + (
        partner_back[:, width].astype(jnp.float32) + partner_back[:, width + 1].astype(jnp.float32)
    )
    sum_high, sum_low = split_bf16(gate_sum)
    ret_extra = jnp.where(
        back_lane == 0,
        sum_high[:, None],
        jnp.where(back_lane == 1, sum_low[:, None], jnp.zeros((), jnp.bfloat16)),
    )
    back = jnp.concatenate([token_sum, ret_extra], axis=1)
    back_width = back.shape[1]
    returned = lax.all_to_all(
        back.reshape(experts, capacity * back_width // LANES, LANES),
        "epc",
        split_axis=0,
        concat_axis=0,
        tiled=True,
    ).reshape(experts * capacity, back_width)
    slots = jnp.arange(experts * capacity, dtype=jnp.int32)[None, None, :]
    select = jnp.any(position.reshape(tok_rows, 2)[:, :, None] == slots, axis=1)
    token_grad = jnp.dot(
        select.astype(jnp.bfloat16), returned[:, :width], preferred_element_type=jnp.float32
    ).astype(jnp.bfloat16)
    returned_gate = returned[:, width].astype(jnp.float32) + returned[:, width + 1].astype(
        jnp.float32
    )
    gated_grad = returned_gate[position]
    gate_grad = (gated_grad / gate_values.reshape(-1)).reshape(tok_rows, 2)
    return (token_grad, gate_grad, down_sum)


def solution(mesh):
    ep_size = mesh.shape["ep"]
    split_mesh = Mesh(
        mesh.devices.reshape(ep_size // 2, 2, mesh.shape["rep"]), ("epc", "core", "rep")
    )
    ep = ("epc", "core")
    return jax.shard_map(
        local,
        mesh=split_mesh,
        in_specs=(
            P(ep + ("rep",), None),
            P(ep + ("rep",), None),
            P(ep + ("rep",), None),
            P(ep + ("rep",), None),
            P("rep", ep),
            P(ep, "rep"),
        ),
        out_specs=(P(ep + ("rep",), None), P(ep + ("rep",), None), P(ep, "rep")),
        check_vma=False,
    )
```
